256 devices in a mesh: row: 64 (over z_hi, y, x), col: 4 (over z_lo, core).
Axes of the slice: x: 4, y: 4, z: 8 (z_hi: 4, z_lo: 2; z = z_hi * 2 + z_lo), core: 2. Of those that a mesh axis runs over, the one named last changes fastest.
Arguments:
- amplitudes: float32 [6400, 12800], P('row', 'col'), may hold values from -6 to 6
- intermediate: float32 [1600, 8192], P('row', 'col'), may hold values from -0.15625 to 0.15625
Outputs:
- cycle_term: float32 [51200, 8192], P('row', 'col')
The draws below stay inside these ranges and needn't reach their ends.
All inputs are finite; a program needn't handle non-finite values.
Results may differ from the reference program's by a relative error of at most 0.00007.
Values sent between devices are 32-bit elements; how exact they have to be, the bound alone decides.
No kernel may reach another device: no remote copies, remote signals or barrier semaphores. Data moves between devices by JAX's collectives and lax.ppermute only.
A program may use at most 128 MiB of HBM per device.

```python
import jax
import jax.numpy as jnp
from jax import lax

O = 40
V = 320
R = 4
KC = 8192
BW = 40


def level_of(key, dims, split, low, top_value):
    factor_of, own = 1.0, jax.random.fold_in(key, 6)
    for position, blocks in split:
        heights = jnp.exp(jax.random.uniform(jax.random.fold_in(own, position), (blocks,), jnp.float32, low / len(split), top_value / len(split)))
        factor_of = factor_of * jnp.repeat(heights, dims[position] // blocks).reshape([-1 if axis == position else 1 for axis in range(len(dims))])
    return factor_of


def noise(stream_key, dims, scale, limit, pieces=(), held_as=jnp.bfloat16):
    result = scale * jax.random.normal(stream_key, dims, jnp.float32)
    if pieces:
        result = result * level_of(stream_key, dims, pieces, -0.22, 0.18)
    return jnp.clip(result, -limit, limit).astype(held_as)


def setup_inputs(seed: int = 0) -> dict:
    key_of = jax.random.split(jax.random.key(seed), 3)
    return {
        "amplitudes": noise(key_of[0], (R * O * O, BW * V), 1.0, 6.0, ((0, 64), (1, 4)), jnp.float32),
        "intermediate": noise(key_of[1], (O * BW, KC), (O * BW) ** -0.5, 0.15625, ((0, 64), (1, 4)), jnp.float32),
    }


def reference(amplitudes, intermediate):
    five_index = amplitudes.reshape(R, O, O, BW, V)
    regrouped = five_index.transpose(4, 0, 1, 3, 2).reshape(V * R * O, BW * O)
    return jnp.dot(regrouped, intermediate, precision=lax.Precision.HIGHEST, preferred_element_type=jnp.float32)
```

```python
import jax
import jax.numpy as jnp
from jax import lax
from jax.sharding import Mesh, PartitionSpec as P

O = 40
V = 320
ROW = ("zh", "y", "x")
COL = ("zl", "core")
CHUNKS = 2


def regroup_local(amplitudes, row_count):
    pair_rows = amplitudes.shape[0]
    b_count = amplitudes.shape[1] // V
    virt_local = V // row_count
    outgoing = amplitudes.reshape(pair_rows, b_count, V).transpose(2, 1, 0)
    received = lax.all_to_all(outgoing, ROW, split_axis=0, concat_axis=2, tiled=True)
    set_rows = received.shape[2] // O
    blocks = received.reshape(virt_local, b_count, set_rows, O).transpose(0, 2, 1, 3)
    return blocks.reshape(virt_local * set_rows, b_count * O)


def ring_zh(part):
    right = [(i, (i + 1) % 4) for i in range(4)]
    left = [(i, (i - 1) % 4) for i in range(4)]
    from_left = lax.ppermute(part, "zh", right)
    from_right = lax.ppermute(part, "zh", left)
    from_far = lax.ppermute(from_left, "zh", right)
    return jnp.concatenate([part, from_right, from_far, from_left], axis=0)


def exchange_col(block):
    zl = lax.axis_index("zl")
    core = lax.axis_index("core")
    zh = lax.axis_index("zh")
    me = zl * 2 + core
    from_zl = lax.ppermute(block, "zl", [(0, 1), (1, 0)])
    pair = jnp.stack([block, from_zl])
    from_core = lax.ppermute(pair, "core", [(0, 1), (1, 0)])
    buf = jnp.zeros((4,) + block.shape, block.dtype)
    for d, piece in ((0, block), (2, from_zl), (1, from_core[0]), (3, from_core[1])):
        buf = lax.dynamic_update_slice(buf, piece[None], (lax.rem(jnp.bitwise_xor(me, d) - zh + 4, 4), 0, 0))
    return buf


def local(amplitudes, intermediate):
    row_count = 64
    block = regroup_local(amplitudes, row_count)
    buf = exchange_col(block)
    rows, width = block.shape
    yx = 16
    piece = width // yx
    regrouped = buf.reshape(4, rows, yx, piece).transpose(1, 2, 0, 3).reshape(rows, 4 * width)
    cols = intermediate.shape[1]
    step = cols // CHUNKS
    outs = []
    for c in range(CHUNKS):
        part = intermediate[:, c * step:(c + 1) * step]
        part = ring_zh(part)
        part = lax.all_gather(part, ("y", "x"), axis=0, tiled=True)
        outs.append(
            jnp.dot(regrouped, part, precision=lax.Precision.HIGH, preferred_element_type=jnp.float32)
        )
    return jnp.concatenate(outs, axis=1)


def solution(mesh):
    devices = mesh.devices.reshape(4, 4, 4, 2, 2)
    fine = Mesh(devices, ROW + COL)
    spec = P(ROW, COL)
    return jax.shard_map(local, mesh=fine, in_specs=(spec, spec), out_specs=spec, check_vma=False)
```

```python
import jax
import jax.numpy as jnp
from jax import lax
from jax.sharding import Mesh, PartitionSpec as P

O = 40
V = 320
ROW = ("zh", "y", "x")
COL = ("zl", "core")
CHUNKS = 2


def regroup_local(amplitudes, row_count):
    pair_rows = amplitudes.shape[0]
    b_count = amplitudes.shape[1] // V
    virt_local = V // row_count
    outgoing = amplitudes.reshape(pair_rows, b_count, V).transpose(2, 1, 0)
    received = lax.all_to_all(outgoing, ROW, split_axis=0, concat_axis=2, tiled=True)
    set_rows = received.shape[2] // O
    blocks = received.reshape(virt_local, b_count, set_rows, O).transpose(0, 2, 1, 3)
    return blocks.reshape(virt_local * set_rows, b_count * O)


def ring_zh(part):
    right = [(i, (i + 1) % 4) for i in range(4)]
    left = [(i, (i - 1) % 4) for i in range(4)]
    from_left = lax.ppermute(part, "zh", right)
    from_right = lax.ppermute(part, "zh", left)
    from_far = lax.ppermute(from_left, "zh", right)
    return jnp.concatenate([part, from_right, from_far, from_left], axis=0)


def exchange_col(block, slots):
    zl = lax.axis_index("zl")
    core = lax.axis_index("core")
    zh = lax.axis_index("zh")
    me = zl * 2 + core
    from_zl = lax.ppermute(block, "zl", [(0, 1), (1, 0)])
    pair = jnp.stack([block, from_zl])
    from_core = lax.ppermute(pair, "core", [(0, 1), (1, 0)])
    by_d = (block, from_core[0], from_zl, from_core[1])
    rows, width = block.shape
    outs = []
    for s in range(4):
        d = jnp.bitwise_xor(me, lax.rem(s + zh, 4))
        pick = jnp.where(d == 0, by_d[0], jnp.where(d == 1, by_d[1], jnp.where(d == 2, by_d[2], by_d[3])))
        outs.append(pick.reshape(rows, slots[0], 1, slots[1]))
    return jnp.concatenate(outs, axis=2).reshape(rows, 4 * width)


def local(amplitudes, intermediate):
    row_count = 64
    block = regroup_local(amplitudes, row_count)
    yx = 16
    piece = intermediate.shape[0]
    regrouped = exchange_col(block, (yx, piece))
    ringed = ring_zh(intermediate)
    cols = intermediate.shape[1]
    step = cols // CHUNKS
    outs = []
    for c in range(CHUNKS):
        part = ringed[:, c * step:(c + 1) * step]
        part = lax.all_gather(part, ("y", "x"), axis=0, tiled=True)
        outs.append(
            jnp.dot(regrouped, part, precision=lax.Precision.HIGH, preferred_element_type=jnp.float32)
        )
    return jnp.concatenate(outs, axis=1)


def solution(mesh):
    devices = mesh.devices.reshape(4, 4, 4, 2, 2)
    fine = Mesh(devices, ROW + COL)
    spec = P(ROW, COL)
    return jax.shard_map(local, mesh=fine, in_specs=(spec, spec), out_specs=spec, check_vma=False)
```

```python
import jax
import jax.numpy as jnp
from jax import lax
from jax.sharding import Mesh, PartitionSpec as P

O = 40
V = 320
ROW = ("zh", "y", "x")
COL = ("zl", "core")
CHUNKS = 4


def regroup_local(amplitudes, row_count):
    pair_rows = amplitudes.shape[0]
    b_count = amplitudes.shape[1] // V
    virt_local = V // row_count
    outgoing = amplitudes.reshape(pair_rows, b_count, V).transpose(2, 1, 0)
    received = lax.all_to_all(outgoing, ROW, split_axis=0, concat_axis=2, tiled=True)
    set_rows = received.shape[2] // O
    blocks = received.reshape(virt_local, b_count, set_rows, O).transpose(0, 2, 1, 3)
    return blocks.reshape(virt_local * set_rows, b_count * O)


def ring_zh(part):
    right = [(i, (i + 1) % 4) for i in range(4)]
    left = [(i, (i - 1) % 4) for i in range(4)]
    from_left = lax.ppermute(part, "zh", right)
    from_right = lax.ppermute(part, "zh", left)
    from_far = lax.ppermute(from_left, "zh", right)
    return jnp.concatenate([part, from_right, from_far, from_left], axis=0)


def exchange_col(block, slots, padded):
    zl = lax.axis_index("zl")
    core = lax.axis_index("core")
    zh = lax.axis_index("zh")
    me = zl * 2 + core
    from_zl = lax.ppermute(block, "zl", [(0, 1), (1, 0)])
    pair = jnp.stack([block, from_zl])
    from_core = lax.ppermute(pair, "core", [(0, 1), (1, 0)])
    by_d = (block, from_core[0], from_zl, from_core[1])
    rows, width = block.shape
    outs = []
    for s in range(4):
        d = jnp.bitwise_xor(me, lax.rem(s + zh, 4))
        pick = jnp.where(d == 0, by_d[0], jnp.where(d == 1, by_d[1], jnp.where(d == 2, by_d[2], by_d[3])))
        outs.append(pick.reshape(rows, slots[0], slots[1]))
    outs.append(jnp.zeros((rows, slots[0], padded - 4 * slots[1]), block.dtype))
    return jnp.concatenate(outs, axis=2).reshape(rows, slots[0] * padded)


def local(amplitudes, intermediate):
    row_count = 64
    block = regroup_local(amplitudes, row_count)
    yx = 16
    piece = intermediate.shape[0]
    ringed = ring_zh(intermediate)
    height = -(-ringed.shape[0] // 8) * 8
    ringed = jnp.pad(ringed, ((0, height - ringed.shape[0]), (0, 0)))
    regrouped = exchange_col(block, (yx, piece), height)
    cols = intermediate.shape[1]
    step = cols // CHUNKS
    outs = []
    for c in range(CHUNKS):
        part = ringed[:, c * step:(c + 1) * step]
        part = lax.all_gather(part, ("y", "x"), axis=0, tiled=True)
        outs.append(
            jnp.dot(regrouped, part, precision=lax.Precision.HIGH, preferred_element_type=jnp.float32)
        )
    return jnp.concatenate(outs, axis=1)


def solution(mesh):
    devices = mesh.devices.reshape(4, 4, 4, 2, 2)
    fine = Mesh(devices, ROW + COL)
    spec = P(ROW, COL)
    return jax.shard_map(local, mesh=fine, in_specs=(spec, spec), out_specs=spec, check_vma=False)
```

```python
import jax
import jax.numpy as jnp
from jax import lax
from jax.sharding import Mesh, PartitionSpec as P

O = 40
V = 320
ROW = ("zh", "y", "x")
COL = ("zl", "core")
CHUNKS = 1


def regroup_local(amplitudes, row_count):
    pair_rows = amplitudes.shape[0]
    b_count = amplitudes.shape[1] // V
    virt_local = V // row_count
    outgoing = amplitudes.reshape(pair_rows, b_count, V).transpose(2, 1, 0)
    received = lax.all_to_all(outgoing, ROW, split_axis=0, concat_axis=2, tiled=True)
    set_rows = received.shape[2] // O
    blocks = received.reshape(virt_local, b_count, set_rows, O).transpose(0, 2, 1, 3)
    return blocks.reshape(virt_local * set_rows, b_count * O)


def ring_zh(part):
    right = [(i, (i + 1) % 4) for i in range(4)]
    left = [(i, (i - 1) % 4) for i in range(4)]
    from_left = lax.ppermute(part, "zh", right)
    from_right = lax.ppermute(part, "zh", left)
    from_far = lax.ppermute(from_left, "zh", right)
    return jnp.concatenate([part, from_right, from_far, from_left], axis=0)


def exchange_col(block, slots):
    zl = lax.axis_index("zl")
    core = lax.axis_index("core")
    zh = lax.axis_index("zh")
    me = zl * 2 + core
    from_zl = lax.ppermute(block, "zl", [(0, 1), (1, 0)])
    pair = jnp.stack([block, from_zl])
    from_core = lax.ppermute(pair, "core", [(0, 1), (1, 0)])
    by_d = (block, from_core[0], from_zl, from_core[1])
    rows, width = block.shape
    outs = []
    for s in range(4):
        d = jnp.bitwise_xor(me, lax.rem(s + zh, 4))
        pick = jnp.where(d == 0, by_d[0], jnp.where(d == 1, by_d[1], jnp.where(d == 2, by_d[2], by_d[3])))
        outs.append(pick.reshape(rows, slots[0], 1, slots[1]))
    return jnp.concatenate(outs, axis=2).reshape(rows, 4 * width)


def local(amplitudes, intermediate):
    row_count = 64
    block = regroup_local(amplitudes, row_count)
    yx = 16
    piece = intermediate.shape[0]
    ringed = ring_zh(intermediate)
    regrouped = exchange_col(block, (yx, piece))
    cols = intermediate.shape[1]
    step = cols // CHUNKS
    outs = []
    for c in range(CHUNKS):
        part = ringed[:, c * step:(c + 1) * step]
        part = lax.all_gather(part, ("y", "x"), axis=0, tiled=True)
        outs.append(
            jnp.dot(regrouped, part, precision=lax.Precision.HIGH, preferred_element_type=jnp.float32)
        )
    return jnp.concatenate(outs, axis=1)


def solution(mesh):
    devices = mesh.devices.reshape(4, 4, 4, 2, 2)
    fine = Mesh(devices, ROW + COL)
    spec = P(ROW, COL)
    return jax.shard_map(local, mesh=fine, in_specs=(spec, spec), out_specs=spec, check_vma=False)
```

```python
import jax
import jax.numpy as jnp
from jax import lax
from jax.sharding import Mesh, PartitionSpec as P

O = 40
V = 320
ROW = ("zh", "y", "x")
COL = ("zl", "core")
CHUNKS = 1


def regroup_local(amplitudes, row_count):
    pair_rows = amplitudes.shape[0]
    b_count = amplitudes.shape[1] // V
    virt_local = V // row_count
    outgoing = amplitudes.reshape(pair_rows, b_count, V).transpose(2, 1, 0)
    received = lax.all_to_all(outgoing, ROW, split_axis=0, concat_axis=2, tiled=True)
    set_rows = received.shape[2] // O
    blocks = received.reshape(virt_local, b_count, set_rows, O).transpose(0, 2, 1, 3)
    return blocks.reshape(virt_local * set_rows, b_count * O)


def ring_zh(part):
    right = [(i, (i + 1) % 4) for i in range(4)]
    left = [(i, (i - 1) % 4) for i in range(4)]
    across = [(i, (i + 2) % 4) for i in range(4)]
    from_left = lax.ppermute(part, "zh", right)
    from_right = lax.ppermute(part, "zh", left)
    from_far = lax.ppermute(part, "zh", across)
    return jnp.stack([part, from_right, from_far, from_left])


def exchange_col(block, slots):
    zl = lax.axis_index("zl")
    core = lax.axis_index("core")
    zh = lax.axis_index("zh")
    me = zl * 2 + core
    from_zl = lax.ppermute(block, "zl", [(0, 1), (1, 0)])
    pair = jnp.stack([block, from_zl])
    from_core = lax.ppermute(pair, "core", [(0, 1), (1, 0)])
    by_d = (block, from_core[0], from_zl, from_core[1])
    rows, width = block.shape
    outs = []
    for s in range(4):
        d = jnp.bitwise_xor(me, lax.rem(s + zh, 4))
        pick = jnp.where(d == 0, by_d[0], jnp.where(d == 1, by_d[1], jnp.where(d == 2, by_d[2], by_d[3])))
        outs.append(pick)
    return jnp.concatenate(outs, axis=1)


def local(amplitudes, intermediate):
    row_count = 64
    block = regroup_local(amplitudes, row_count)
    yx = 16
    piece = intermediate.shape[0]
    ringed = ring_zh(intermediate)
    regrouped = exchange_col(block, (yx, piece))
    cols = intermediate.shape[1]
    step = cols // CHUNKS
    outs = []
    for c in range(CHUNKS):
        part = ringed[:, :, c * step:(c + 1) * step]
        part = lax.all_gather(part, ("y", "x"), axis=1, tiled=True).reshape(-1, step)
        outs.append(
            jnp.dot(regrouped, part, precision=lax.Precision.HIGH, preferred_element_type=jnp.float32)
        )
    return jnp.concatenate(outs, axis=1)


def solution(mesh):
    devices = mesh.devices.reshape(4, 4, 4, 2, 2)
    fine = Mesh(devices, ROW + COL)
    spec = P(ROW, COL)
    return jax.shard_map(local, mesh=fine, in_specs=(spec, spec), out_specs=spec, check_vma=False)
```

```python
import jax
import jax.numpy as jnp
from jax import lax
from jax.sharding import Mesh, PartitionSpec as P

O = 40
V = 320
ROW = ("zh", "y", "x")
COL = ("zl", "core")
CHUNKS = 1


def regroup_local(amplitudes, row_count):
    pair_rows = amplitudes.shape[0]
    b_count = amplitudes.shape[1] // V
    virt_local = V // row_count
    outgoing = amplitudes.reshape(pair_rows, b_count, V).transpose(2, 1, 0)
    received = lax.all_to_all(outgoing, ROW, split_axis=0, concat_axis=2, tiled=True)
    set_rows = received.shape[2] // O
    blocks = received.reshape(virt_local, b_count, set_rows, O).transpose(0, 2, 1, 3)
    return blocks.reshape(virt_local * set_rows, b_count * O)


def ring_zh(part):
    right = [(i, (i + 1) % 4) for i in range(4)]
    left = [(i, (i - 1) % 4) for i in range(4)]
    across = [(i, (i + 2) % 4) for i in range(4)]
    from_left = lax.ppermute(part, "zh", right)
    from_right = lax.ppermute(part, "zh", left)
    from_far = lax.ppermute(part, "zh", across)
    return jnp.stack([part, from_right, from_far, from_left])


def exchange_col(block, slots):
    zl = lax.axis_index("zl")
    core = lax.axis_index("core")
    zh = lax.axis_index("zh")
    me = zl * 2 + core
    swap = [(0, 1), (1, 0)]
    from_zl = lax.ppermute(block, "zl", swap)
    from_core = lax.ppermute(block, "core", swap)
    from_both = lax.ppermute(from_zl, "core", swap)
    by_d = (block, from_core, from_zl, from_both)
    rows, width = block.shape
    outs = []
    for s in range(4):
        d = jnp.bitwise_xor(me, lax.rem(s + zh, 4))
        pick = jnp.where(d == 0, by_d[0], jnp.where(d == 1, by_d[1], jnp.where(d == 2, by_d[2], by_d[3])))
        outs.append(pick)
    return jnp.concatenate(outs, axis=1)


def local(amplitudes, intermediate):
    row_count = 64
    block = regroup_local(amplitudes, row_count)
    yx = 16
    piece = intermediate.shape[0]
    ringed = ring_zh(intermediate)
    regrouped = exchange_col(block, (yx, piece))
    cols = intermediate.shape[1]
    step = cols // CHUNKS
    outs = []
    for c in range(CHUNKS):
        part = ringed[:, :, c * step:(c + 1) * step]
        part = lax.all_gather(part, ("y", "x"), axis=1, tiled=True).reshape(-1, step)
        outs.append(
            jnp.dot(regrouped, part, precision=lax.Precision.HIGH, preferred_element_type=jnp.float32)
        )
    return jnp.concatenate(outs, axis=1)


def solution(mesh):
    devices = mesh.devices.reshape(4, 4, 4, 2, 2)
    fine = Mesh(devices, ROW + COL)
    spec = P(ROW, COL)
    return jax.shard_map(local, mesh=fine, in_specs=(spec, spec), out_specs=spec, check_vma=False)
```

```python
import jax
import jax.numpy as jnp
from jax import lax
from jax.sharding import Mesh, PartitionSpec as P

O = 40
V = 320
ROW = ("zh", "y", "x")
COL = ("zl", "core")
CHUNKS = 1


def regroup_local(amplitudes, row_count):
    pair_rows = amplitudes.shape[0]
    b_count = amplitudes.shape[1] // V
    virt_local = V // row_count
    outgoing = amplitudes.reshape(pair_rows, b_count, V).transpose(2, 1, 0)
    received = lax.all_to_all(outgoing, ROW, split_axis=0, concat_axis=2, tiled=True)
    set_rows = received.shape[2] // O
    blocks = received.reshape(virt_local, b_count, set_rows, O).transpose(0, 2, 1, 3)
    return blocks.reshape(virt_local * set_rows, b_count * O)


def ring_zh(part):
    right = [(i, (i + 1) % 4) for i in range(4)]
    left = [(i, (i - 1) % 4) for i in range(4)]
    across = [(i, (i + 2) % 4) for i in range(4)]
    from_left = lax.ppermute(part, "zh", right)
    from_right = lax.ppermute(part, "zh", left)
    from_far = lax.ppermute(part, "zh", across)
    return jnp.stack([part, from_right, from_far, from_left])


def exchange_col(block, slots):
    zl = lax.axis_index("zl")
    core = lax.axis_index("core")
    zh = lax.axis_index("zh")
    me = zl * 2 + core
    swap = [(0, 1), (1, 0)]
    from_zl = lax.ppermute(block, "zl", swap)
    from_core = lax.ppermute(block, "core", swap)
    from_both = lax.ppermute(from_zl, "core", swap)
    by_d = (block, from_core, from_zl, from_both)
    rows, width = block.shape
    outs = []
    for s in range(4):
        d = jnp.bitwise_xor(me, lax.rem(s + zh, 4))
        pick = jnp.where(d == 0, by_d[0], jnp.where(d == 1, by_d[1], jnp.where(d == 2, by_d[2], by_d[3])))
        outs.append(pick)
    return jnp.stack(outs, axis=1)


def local(amplitudes, intermediate):
    row_count = 64
    block = regroup_local(amplitudes, row_count)
    yx = 16
    piece = intermediate.shape[0]
    ringed = ring_zh(intermediate)
    regrouped = exchange_col(block, (yx, piece))
    cols = intermediate.shape[1]
    step = cols // CHUNKS
    outs = []
    for c in range(CHUNKS):
        part = ringed[:, :, c * step:(c + 1) * step]
        part = lax.all_gather(part, ("y", "x"), axis=1, tiled=True)
        outs.append(
            lax.dot_general(
                regrouped, part, (((1, 2), (0, 1)), ((), ())),
                precision=lax.Precision.HIGH, preferred_element_type=jnp.float32,
            )
        )
    return jnp.concatenate(outs, axis=1)


def solution(mesh):
    devices = mesh.devices.reshape(4, 4, 4, 2, 2)
    fine = Mesh(devices, ROW + COL)
    spec = P(ROW, COL)
    return jax.shard_map(local, mesh=fine, in_specs=(spec, spec), out_specs=spec, check_vma=False)
```

```python
import jax
import jax.numpy as jnp
from jax import lax
from jax.sharding import Mesh, PartitionSpec as P

O = 40
V = 320
ROW = ("zh", "y", "x")
COL = ("zl", "core")
CHUNKS = 1


def regroup_local(amplitudes, row_count):
    pair_rows = amplitudes.shape[0]
    b_count = amplitudes.shape[1] // V
    virt_local = V // row_count
    outgoing = amplitudes.reshape(pair_rows, b_count, V).transpose(2, 1, 0).reshape(V, b_count * pair_rows)
    received = lax.all_to_all(outgoing, ROW, split_axis=0, concat_axis=0, tiled=True)
    received = received.reshape(row_count, virt_local, b_count, pair_rows).transpose(1, 2, 0, 3)
    set_rows = row_count * pair_rows // O
    blocks = received.reshape(virt_local, b_count, set_rows, O).transpose(0, 2, 1, 3)
    return blocks.reshape(virt_local * set_rows, b_count * O)


def ring_zh(part):
    right = [(i, (i + 1) % 4) for i in range(4)]
    left = [(i, (i - 1) % 4) for i in range(4)]
    across = [(i, (i + 2) % 4) for i in range(4)]
    from_left = lax.ppermute(part, "zh", right)
    from_right = lax.ppermute(part, "zh", left)
    from_far = lax.ppermute(part, "zh", across)
    return jnp.stack([part, from_right, from_far, from_left])


def exchange_col(block, slots):
    zl = lax.axis_index("zl")
    core = lax.axis_index("core")
    zh = lax.axis_index("zh")
    me = zl * 2 + core
    swap = [(0, 1), (1, 0)]
    from_zl = lax.ppermute(block, "zl", swap)
    from_core = lax.ppermute(block, "core", swap)
    from_both = lax.ppermute(from_zl, "core", swap)
    by_d = (block, from_core, from_zl, from_both)
    rows, width = block.shape
    outs = []
    for s in range(4):
        d = jnp.bitwise_xor(me, lax.rem(s + zh, 4))
        pick = jnp.where(d == 0, by_d[0], jnp.where(d == 1, by_d[1], jnp.where(d == 2, by_d[2], by_d[3])))
        outs.append(pick)
    return jnp.stack(outs, axis=1)


def local(amplitudes, intermediate):
    row_count = 64
    block = regroup_local(amplitudes, row_count)
    yx = 16
    piece = intermediate.shape[0]
    ringed = ring_zh(intermediate)
    regrouped = exchange_col(block, (yx, piece))
    cols = intermediate.shape[1]
    step = cols // CHUNKS
    outs = []
    for c in range(CHUNKS):
        part = ringed[:, :, c * step:(c + 1) * step]
        part = lax.all_gather(part, ("y", "x"), axis=1, tiled=True)
        outs.append(
            lax.dot_general(
                regrouped, part, (((1, 2), (0, 1)), ((), ())),
                precision=lax.Precision.HIGH, preferred_element_type=jnp.float32,
            )
        )
    return jnp.concatenate(outs, axis=1)


def solution(mesh):
    devices = mesh.devices.reshape(4, 4, 4, 2, 2)
    fine = Mesh(devices, ROW + COL)
    spec = P(ROW, COL)
    return jax.shard_map(local, mesh=fine, in_specs=(spec, spec), out_specs=spec, check_vma=False)
```
